256 devices in a mesh: dp: 16 (over z_lo, x), tensor: 16 (over z_hi, y, core).
Axes of the slice: x: 4, y: 4, z: 8 (z_hi: 2, z_lo: 4; z = z_hi * 4 + z_lo), core: 2. Of those that a mesh axis runs over, the one named last changes fastest.
Arguments:
- cotangent: bfloat16 [8192, 4096], P(('dp', 'tensor')), may hold values from -6 to 6
- gate: bfloat16 [8192, 14336], P('dp', 'tensor'), may hold values from -8 to 8
- up: bfloat16 [8192, 14336], P('dp', 'tensor'), may hold values from -6 to 6
- w_down: bfloat16 [4, 14336, 4096], P(None, 'tensor', 'dp'), may hold values from -0.03125 to 0.03125
- language: int32 [16], replicated, may hold values from 0 to 3
Outputs:
- d_gate: bfloat16 [8192, 14336], P('dp', 'tensor')
- d_up: bfloat16 [8192, 14336], P('dp', 'tensor')
- d_weight: float32 [4, 14336, 4096], P(None, 'tensor', 'dp')
The draws below stay inside these ranges and needn't reach their ends.
All inputs are finite; a program needn't handle non-finite values.
Results may differ from the reference program's by a relative error of at most 0.0029.
Values may be sent and summed in bfloat16 or wider, within the bound.
No kernel may reach another device: no remote copies, remote signals or barrier semaphores. Data moves between devices by JAX's collectives and lax.ppermute only.
A program may use at most 128 MiB of HBM per device.

```python
import jax
import jax.numpy as jnp
from jax import lax

D = 4096
FF = 14336
LANGS = 4
TOK_GRP = 512
GROUPS = 16
TOKENS = 8192
N_DP = 16


def touch_ends(values, key, least, largest):
    place = [jax.random.randint(jax.random.fold_in(key, axis), (), 0, length) for axis, length in enumerate(values.shape)]
    longest = values.shape.index(max(values.shape))
    next_to = place[:longest] + [(place[longest] + 1) % values.shape[longest]] + place[longest + 1:]
    return values.at[tuple(place)].set(least).at[tuple(next_to)].set(largest)


def block_scale(stream_key, dims, pieces, low, high):
    def one(position, shards_of):
        heights = jax.random.uniform(jax.random.fold_in(jax.random.fold_in(stream_key, 6), position), (shards_of,), jnp.float32, low / len(pieces), high / len(pieces))
        return jnp.repeat(jnp.exp(heights), dims[position] // shards_of).reshape((-1,) + (1,) * (len(dims) - position - 1))

    factor_of = one(*pieces[0])
    for cut in pieces[1:]:
        factor_of = factor_of * one(*cut)
    return factor_of


def normal_values(rng, dims, width, most, pieces=(), held_as=jnp.bfloat16):
    drawn = width * jax.random.normal(rng, dims, jnp.float32)
    if pieces:
        drawn = drawn * block_scale(rng, dims, pieces, -0.22, 0.18)
    return jnp.clip(drawn, -most, most).astype(held_as)


def setup_inputs(seed: int = 0) -> dict:
    key_of = jax.random.split(jax.random.key(seed), 6)
    cotangent = normal_values(key_of[0], (TOKENS, D), 1.0, 6.0, ((0, 256),))
    gate = normal_values(key_of[1], (TOKENS, FF), 2.0, 8.0, ((0, 16), (1, 16)))
    up = normal_values(key_of[2], (TOKENS, FF), 1.0, 6.0, ((0, 16), (1, 16)))
    w_down = normal_values(key_of[3], (LANGS, FF, D), (2 * FF) ** -0.5, 0.03125, ((1, 16), (2, 16)))
    language = touch_ends(jax.random.randint(key_of[4], (GROUPS,), 0, LANGS), jax.random.fold_in(key_of[4], 1), 0, LANGS - 1).astype(jnp.int32)
    return {"cotangent": cotangent, "gate": gate, "up": up, "w_down": w_down, "language": language}


def reference(cotangent, gate, up, w_down, language):
    cot3 = cotangent.reshape(N_DP, TOK_GRP, D)
    gate3 = gate.reshape(N_DP, TOK_GRP, FF)
    up3 = up.reshape(N_DP, TOK_GRP, FF)

    def step(accum, items):
        cot_g, gate_g, up_g, lang_g = items
        weights = w_down[lang_g]
        gate_f = gate_g.astype(jnp.float32)
        up_f = up_g.astype(jnp.float32)
        sig = jax.nn.sigmoid(gate_f)
        act = gate_f * sig
        hidden = (act * up_f).astype(jnp.bfloat16)
        d_hidden = jnp.dot(cot_g, weights.T, preferred_element_type=jnp.float32)
        d_up_g = (d_hidden * act).astype(jnp.bfloat16)
        d_gate_g = (d_hidden * up_f * sig * (1.0 + gate_f * (1.0 - sig))).astype(jnp.bfloat16)
        part = jnp.dot(hidden.T, cot_g, preferred_element_type=jnp.float32)
        accum = accum.at[lang_g].add(part)
        return accum, (d_gate_g, d_up_g)

    init = jnp.zeros((LANGS, FF, D), jnp.float32)
    d_weight, outs = lax.scan(step, init, (cot3, gate3, up3, language))
    d_gate = outs[0].reshape(N_DP * TOK_GRP, FF)
    d_up = outs[1].reshape(N_DP * TOK_GRP, FF)
    return d_gate, d_up, d_weight
```

```python
import jax
import jax.numpy as jnp
from jax import lax
from jax.sharding import Mesh
from jax.sharding import PartitionSpec as P

DP = ("zl", "x")
TP = ("zh", "y", "c")


def shards(cotangent, gate, up, w_down, language):
    groups = lax.axis_size(DP)
    variants = w_down.shape[0]
    ff_dev = w_down.shape[1]
    feat_dev = w_down.shape[2]
    rows_dev, feats = cotangent.shape
    cores = lax.axis_size("c")
    chip_rows = lax.all_gather(cotangent, ("zh", "y"), axis=0, tiled=False)
    both = lax.all_gather(chip_rows, "c", axis=0, tiled=False)
    out_rows = jnp.swapaxes(both, 0, 1).reshape(-1, feats)
    gate_f = gate.astype(jnp.float32)
    up_f = up.astype(jnp.float32)
    sig = jax.nn.sigmoid(gate_f)
    act = gate_f * sig
    hidden = (act * up_f).astype(jnp.bfloat16)
    slabs = jnp.take(w_down, language, axis=0)
    received = lax.all_to_all(slabs, DP, split_axis=0, concat_axis=2, tiled=True)
    weights = received[0]
    d_hidden = lax.dot_general(
        out_rows, weights, (((1,), (1,)), ((), ())), preferred_element_type=jnp.float32
    )
    d_up = (d_hidden * act).astype(jnp.bfloat16)
    d_gate = (d_hidden * up_f * sig * (1.0 + gate_f * (1.0 - sig))).astype(jnp.bfloat16)
    selector = (language[None, :] == jnp.arange(variants, dtype=jnp.int32)[:, None]).astype(
        jnp.bfloat16
    )
    partial_term = lax.dot_general(
        hidden, out_rows, (((0,), (0,)), ((), ())), preferred_element_type=jnp.float32
    ).astype(jnp.bfloat16)
    pieces = lax.all_to_all(
        partial_term.reshape(ff_dev, groups, feat_dev),
        DP,
        split_axis=1,
        concat_axis=1,
        tiled=True,
    )
    d_weight = jnp.einsum("lg,fgd->lfd", selector, pieces, preferred_element_type=jnp.float32)
    return (d_gate, d_up, d_weight)


def solution(mesh):
    sub = Mesh(mesh.devices.reshape(4, 4, 2, 4, 2), DP + TP)
    return jax.shard_map(
        shards,
        mesh=sub,
        in_specs=(
            P(DP + TP, None),
            P(DP, TP),
            P(DP, TP),
            P(None, TP, DP),
            P(),
        ),
        out_specs=(P(DP, TP), P(DP, TP), P(None, TP, DP)),
        check_vma=False,
    )
```

```python
import jax
import jax.numpy as jnp
from jax import lax
from jax.sharding import Mesh
from jax.sharding import PartitionSpec as P

DP = ("zl", "x")
TP = ("zh", "y", "c")


def shards(cotangent, gate, up, w_down, language):
    groups = lax.axis_size(DP)
    variants = w_down.shape[0]
    ff_dev = w_down.shape[1]
    feat_dev = w_down.shape[2]
    rows_dev, feats = cotangent.shape
    cores = lax.axis_size("c")
    partner = lax.ppermute(cotangent, "zh", [(0, 1), (1, 0)])
    first = lax.axis_index("zh") == 0
    pair = jnp.where(first, jnp.stack([cotangent, partner]), jnp.stack([partner, cotangent]))
    ring = lax.axis_size("y")
    me_y = lax.axis_index("y")
    got = [pair]
    for shift in range(1, ring):
        got.append(lax.ppermute(pair, "y", [(i, (i + shift) % ring) for i in range(ring)]))
    by_y = jnp.stack(got)
    order = (me_y - jnp.arange(ring)) % ring
    by_y = jnp.take(by_y, jnp.argsort(order), axis=0, mode="clip")
    other = lax.ppermute(by_y, "c", [(0, 1), (1, 0)])
    first_c = lax.axis_index("c") == 0
    both = jnp.where(first_c, jnp.stack([by_y, other]), jnp.stack([other, by_y]))
    out_rows = jnp.transpose(both, (2, 1, 0, 3, 4)).reshape(-1, feats)
    gate_f = gate.astype(jnp.float32)
    up_f = up.astype(jnp.float32)
    sig = jax.nn.sigmoid(gate_f)
    act = gate_f * sig
    hidden = (act * up_f).astype(jnp.bfloat16)
    slabs = jnp.take(w_down, language, axis=0, mode="clip")
    received = lax.all_to_all(slabs, DP, split_axis=0, concat_axis=2, tiled=True)
    weights = received[0]
    d_hidden = lax.dot_general(
        out_rows, weights, (((1,), (1,)), ((), ())), preferred_element_type=jnp.float32
    )
    d_up = (d_hidden * act).astype(jnp.bfloat16)
    d_gate = (d_hidden * up_f * sig * (1.0 + gate_f * (1.0 - sig))).astype(jnp.bfloat16)
    selector = (language[None, :] == jnp.arange(variants, dtype=jnp.int32)[:, None]).astype(
        jnp.bfloat16
    )
    partial_term = lax.dot_general(
        hidden, out_rows, (((0,), (0,)), ((), ())), preferred_element_type=jnp.float32
    ).astype(jnp.bfloat16)
    pieces = lax.all_to_all(
        partial_term.reshape(ff_dev, groups, feat_dev),
        DP,
        split_axis=1,
        concat_axis=1,
        tiled=True,
    )
    d_weight = jnp.einsum("lg,fgd->lfd", selector, pieces, preferred_element_type=jnp.float32)
    return (d_gate, d_up, d_weight)


def solution(mesh):
    sub = Mesh(mesh.devices.reshape(4, 4, 2, 4, 2), DP + TP)
    return jax.shard_map(
        shards,
        mesh=sub,
        in_specs=(
            P(DP + TP, None),
            P(DP, TP),
            P(DP, TP),
            P(None, TP, DP),
            P(),
        ),
        out_specs=(P(DP, TP), P(DP, TP), P(None, TP, DP)),
        check_vma=False,
    )
```

```python
import jax
import jax.numpy as jnp
from jax import lax
from jax.sharding import Mesh
from jax.sharding import PartitionSpec as P

DP = ("zl", "x")
TP = ("zh", "y", "c")


def shards(cotangent, gate, up, w_down, language):
    groups = lax.axis_size(DP)
    variants = w_down.shape[0]
    ff_dev = w_down.shape[1]
    feat_dev = w_down.shape[2]
    rows_dev, feats = cotangent.shape
    cores = lax.axis_size("c")
    partner = lax.ppermute(cotangent, "zh", [(0, 1), (1, 0)])
    slabs = jnp.take(w_down, language, axis=0, mode="clip")
    partner, slabs = lax.optimization_barrier((partner, slabs))
    first = lax.axis_index("zh") == 0
    pair = jnp.where(first, jnp.stack([cotangent, partner]), jnp.stack([partner, cotangent]))
    ring = lax.axis_size("y")
    me_y = lax.axis_index("y")
    got = [pair]
    for shift in range(1, ring):
        got.append(lax.ppermute(pair, "y", [(i, (i + shift) % ring) for i in range(ring)]))
    by_y = jnp.stack(got)
    order = (me_y - jnp.arange(ring)) % ring
    by_y = jnp.take(by_y, jnp.argsort(order), axis=0, mode="clip")
    other = lax.ppermute(by_y, "c", [(0, 1), (1, 0)])
    first_c = lax.axis_index("c") == 0
    both = jnp.where(first_c, jnp.stack([by_y, other]), jnp.stack([other, by_y]))
    out_rows = jnp.transpose(both, (2, 1, 0, 3, 4)).reshape(-1, feats)
    gate_f = gate.astype(jnp.float32)
    up_f = up.astype(jnp.float32)
    sig = jax.nn.sigmoid(gate_f)
    act = gate_f * sig
    hidden = (act * up_f).astype(jnp.bfloat16)
    received = lax.all_to_all(slabs, DP, split_axis=0, concat_axis=2, tiled=True)
    weights = received[0]
    d_hidden = lax.dot_general(
        out_rows, weights, (((1,), (1,)), ((), ())), preferred_element_type=jnp.float32
    )
    d_up = (d_hidden * act).astype(jnp.bfloat16)
    d_gate = (d_hidden * up_f * sig * (1.0 + gate_f * (1.0 - sig))).astype(jnp.bfloat16)
    selector = (language[None, :] == jnp.arange(variants, dtype=jnp.int32)[:, None]).astype(
        jnp.bfloat16
    )
    partial_term = lax.dot_general(
        hidden, out_rows, (((0,), (0,)), ((), ())), preferred_element_type=jnp.float32
    ).astype(jnp.bfloat16)
    pieces = lax.all_to_all(
        partial_term.reshape(ff_dev, groups, feat_dev),
        DP,
        split_axis=1,
        concat_axis=1,
        tiled=True,
    )
    d_weight = jnp.einsum("lg,fgd->lfd", selector, pieces, preferred_element_type=jnp.float32)
    return (d_gate, d_up, d_weight)


def solution(mesh):
    sub = Mesh(mesh.devices.reshape(4, 4, 2, 4, 2), DP + TP)
    return jax.shard_map(
        shards,
        mesh=sub,
        in_specs=(
            P(DP + TP, None),
            P(DP, TP),
            P(DP, TP),
            P(None, TP, DP),
            P(),
        ),
        out_specs=(P(DP, TP), P(DP, TP), P(None, TP, DP)),
        check_vma=False,
    )
```

```python
import jax
import jax.numpy as jnp
from jax import lax
from jax.sharding import Mesh
from jax.sharding import PartitionSpec as P

DP = ("zh2", "zl2", "x")
HALF = ("zl2", "x")
TP = ("zh", "y", "c")


def shards(cotangent, gate, up, w_down, language):
    groups = lax.axis_size(DP)
    variants = w_down.shape[0]
    ff_dev = w_down.shape[1]
    feat_dev = w_down.shape[2]
    rows_dev, feats = cotangent.shape
    cores = lax.axis_size("c")
    partner = lax.ppermute(cotangent, "zh", [(0, 1), (1, 0)])
    half = lax.axis_size(HALF)
    side = lax.axis_index("zh2")
    lang = language.reshape(2, half)
    own_langs = jnp.take(lang, side, axis=0, mode="clip")
    own_slabs = jnp.take(w_down, own_langs, axis=0, mode="clip")
    partner, own_slabs = lax.optimization_barrier((partner, own_slabs))
    near = lax.all_to_all(own_slabs, HALF, split_axis=0, concat_axis=0, tiled=True)
    block = lax.ppermute(w_down, "zh2", [(0, 1), (1, 0)])
    relay = jnp.take(block, own_langs, axis=0, mode="clip")
    far = lax.all_to_all(relay, HALF, split_axis=0, concat_axis=0, tiled=True)
    first = lax.axis_index("zh") == 0
    pair = jnp.where(first, jnp.stack([cotangent, partner]), jnp.stack([partner, cotangent]))
    ring = lax.axis_size("y")
    me_y = lax.axis_index("y")
    got = [pair]
    for shift in range(1, ring):
        got.append(lax.ppermute(pair, "y", [(i, (i + shift) % ring) for i in range(ring)]))
    by_y = jnp.stack(got)
    order = (me_y - jnp.arange(ring)) % ring
    by_y = jnp.take(by_y, jnp.argsort(order), axis=0, mode="clip")
    other = lax.ppermute(by_y, "c", [(0, 1), (1, 0)])
    first_c = lax.axis_index("c") == 0
    both = jnp.where(first_c, jnp.stack([by_y, other]), jnp.stack([other, by_y]))
    out_rows = jnp.transpose(both, (2, 1, 0, 3, 4)).reshape(-1, feats)
    gate_f = gate.astype(jnp.float32)
    up_f = up.astype(jnp.float32)
    sig = jax.nn.sigmoid(gate_f)
    act = gate_f * sig
    hidden = (act * up_f).astype(jnp.bfloat16)
    rows3 = out_rows.reshape(out_rows.shape[0], 2, half, feat_dev)
    cot_near = jnp.take(rows3, side, axis=1, mode="clip")
    cot_far = jnp.take(rows3, 1 - side, axis=1, mode="clip")
    d_hidden = jnp.einsum(
        "tsd,sfd->tf", cot_near, near, preferred_element_type=jnp.float32
    ) + jnp.einsum("tsd,sfd->tf", cot_far, far, preferred_element_type=jnp.float32)
    d_up = (d_hidden * act).astype(jnp.bfloat16)
    d_gate = (d_hidden * up_f * sig * (1.0 + gate_f * (1.0 - sig))).astype(jnp.bfloat16)
    selector = (language[None, :] == jnp.arange(variants, dtype=jnp.int32)[:, None]).astype(
        jnp.bfloat16
    )
    partial_term = lax.dot_general(
        hidden, out_rows, (((0,), (0,)), ((), ())), preferred_element_type=jnp.float32
    ).astype(jnp.bfloat16)
    pieces = lax.all_to_all(
        partial_term.reshape(ff_dev, groups, feat_dev),
        DP,
        split_axis=1,
        concat_axis=1,
        tiled=True,
    )
    d_weight = jnp.einsum("lg,fgd->lfd", selector, pieces, preferred_element_type=jnp.float32)
    return (d_gate, d_up, d_weight)


def solution(mesh):
    sub = Mesh(mesh.devices.reshape(2, 2, 4, 2, 4, 2), DP + TP)
    return jax.shard_map(
        shards,
        mesh=sub,
        in_specs=(
            P(DP + TP, None),
            P(DP, TP),
            P(DP, TP),
            P(None, TP, DP),
            P(),
        ),
        out_specs=(P(DP, TP), P(DP, TP), P(None, TP, DP)),
        check_vma=False,
    )
```

```python
import jax
import jax.numpy as jnp
from jax import lax
from jax.sharding import Mesh
from jax.sharding import PartitionSpec as P

DP = ("zh2", "zl2", "x")
HALF = ("zl2", "x")
TP = ("zh", "y", "c")


def shards(cotangent, gate, up, w_down, language):
    groups = lax.axis_size(DP)
    variants = w_down.shape[0]
    ff_dev = w_down.shape[1]
    feat_dev = w_down.shape[2]
    rows_dev, feats = cotangent.shape
    cores = lax.axis_size("c")
    partner = lax.ppermute(cotangent, "zh", [(0, 1), (1, 0)])
    half = lax.axis_size(HALF)
    side = lax.axis_index("zh2")
    lang = language.reshape(2, half)
    own_langs = jnp.take(lang, side, axis=0, mode="clip")
    own_slabs = jnp.take(w_down, own_langs, axis=0, mode="clip")
    partner, own_slabs = lax.optimization_barrier((partner, own_slabs))
    near = lax.all_to_all(own_slabs, HALF, split_axis=0, concat_axis=0, tiled=True)
    block = lax.ppermute(w_down, "zh2", [(0, 1), (1, 0)])
    relay = jnp.take(block, own_langs, axis=0, mode="clip")
    far = lax.all_to_all(relay, HALF, split_axis=0, concat_axis=0, tiled=True)
    first = lax.axis_index("zh") == 0
    pair = jnp.where(first, jnp.stack([cotangent, partner]), jnp.stack([partner, cotangent]))
    ring = lax.axis_size("y")
    me_y = lax.axis_index("y")
    got = [pair]
    for shift in range(1, ring):
        got.append(lax.ppermute(pair, "y", [(i, (i + shift) % ring) for i in range(ring)]))
    by_y = jnp.stack(got)
    order = (me_y - jnp.arange(ring)) % ring
    by_y = jnp.take(by_y, jnp.argsort(order), axis=0, mode="clip")
    other = lax.ppermute(by_y, "c", [(0, 1), (1, 0)])
    first_c = lax.axis_index("c") == 0
    both = jnp.where(first_c, jnp.stack([by_y, other]), jnp.stack([other, by_y]))
    out_rows = jnp.transpose(both, (2, 1, 0, 3, 4)).reshape(-1, feats)
    gate_f = gate.astype(jnp.float32)
    up_f = up.astype(jnp.float32)
    sig = jax.nn.sigmoid(gate_f)
    act = gate_f * sig
    hidden = (act * up_f).astype(jnp.bfloat16)
    rows3 = out_rows.reshape(out_rows.shape[0], 2, half, feat_dev)
    cot_near = jnp.take(rows3, side, axis=1, mode="clip")
    cot_far = jnp.take(rows3, 1 - side, axis=1, mode="clip")
    d_hidden = jnp.einsum(
        "tsd,sfd->tf", cot_near, near, preferred_element_type=jnp.float32
    ) + jnp.einsum("tsd,sfd->tf", cot_far, far, preferred_element_type=jnp.float32)
    d_up = (d_hidden * act).astype(jnp.bfloat16)
    d_gate = (d_hidden * up_f * sig * (1.0 + gate_f * (1.0 - sig))).astype(jnp.bfloat16)
    rows_g = out_rows.reshape(out_rows.shape[0], groups, feat_dev)
    pieces = jnp.einsum(
        "tf,tgd->gfd", hidden, rows_g, preferred_element_type=jnp.float32
    ).astype(jnp.bfloat16)
    me = lax.axis_index(DP)
    got = [jnp.take(pieces, me, axis=0, mode="clip")]
    for shift in range(1, groups):
        piece = jnp.take(pieces, (me + shift) % groups, axis=0, mode="clip")
        got.append(
            lax.ppermute(piece, DP, [(i, (i + shift) % groups) for i in range(groups)])
        )
    source = (me - jnp.arange(groups)) % groups
    selector = (
        jnp.take(language, source, mode="clip")[None, :]
        == jnp.arange(variants, dtype=jnp.int32)[:, None]
    ).astype(jnp.bfloat16)
    d_weight = jnp.einsum(
        "lk,kfd->lfd", selector, jnp.stack(got), preferred_element_type=jnp.float32
    )
    return (d_gate, d_up, d_weight)


def solution(mesh):
    sub = Mesh(mesh.devices.reshape(2, 2, 4, 2, 4, 2), DP + TP)
    return jax.shard_map(
        shards,
        mesh=sub,
        in_specs=(
            P(DP + TP, None),
            P(DP, TP),
            P(DP, TP),
            P(None, TP, DP),
            P(),
        ),
        out_specs=(P(DP, TP), P(DP, TP), P(None, TP, DP)),
        check_vma=False,
    )
```

```python
import jax
import jax.numpy as jnp
from jax import lax
from jax.sharding import Mesh
from jax.sharding import PartitionSpec as P

DP = ("zh2", "zl2", "x")
HALF = ("zl2", "x")
TP = ("zh", "y", "c")


def shards(cotangent, gate, up, w_down, language):
    groups = lax.axis_size(DP)
    variants = w_down.shape[0]
    ff_dev = w_down.shape[1]
    feat_dev = w_down.shape[2]
    rows_dev, feats = cotangent.shape
    cores = lax.axis_size("c")
    partner = lax.ppermute(cotangent, "zh", [(0, 1), (1, 0)])
    half = lax.axis_size(HALF)
    side = lax.axis_index("zh2")
    lang = language.reshape(2, half)
    own_langs = jnp.take(lang, side, axis=0, mode="clip")
    own_slabs = jnp.take(w_down, own_langs, axis=0, mode="clip")
    partner, own_slabs = lax.optimization_barrier((partner, own_slabs))
    near = lax.all_to_all(own_slabs, HALF, split_axis=0, concat_axis=0, tiled=True)
    block = lax.ppermute(w_down, "zh2", [(0, 1), (1, 0)])
    relay = jnp.take(block, own_langs, axis=0, mode="clip")
    me_h = lax.axis_index(HALF)
    far = [jnp.take(relay, me_h, axis=0, mode="clip")]
    for shift in range(1, half):
        slab = jnp.take(relay, (me_h + shift) % half, axis=0, mode="clip")
        far.append(lax.ppermute(slab, HALF, [(i, (i + shift) % half) for i in range(half)]))
    far = jnp.stack(far)
    far_src = (me_h - jnp.arange(half)) % half
    first = lax.axis_index("zh") == 0
    pair = jnp.where(first, jnp.stack([cotangent, partner]), jnp.stack([partner, cotangent]))
    ring = lax.axis_size("y")
    me_y = lax.axis_index("y")
    got = [pair]
    for shift in range(1, ring):
        got.append(lax.ppermute(pair, "y", [(i, (i + shift) % ring) for i in range(ring)]))
    by_y = jnp.stack(got)
    order = (me_y - jnp.arange(ring)) % ring
    by_y = jnp.take(by_y, jnp.argsort(order), axis=0, mode="clip")
    other = lax.ppermute(by_y, "c", [(0, 1), (1, 0)])
    first_c = lax.axis_index("c") == 0
    both = jnp.where(first_c, jnp.stack([by_y, other]), jnp.stack([other, by_y]))
    out_rows = jnp.transpose(both, (2, 1, 0, 3, 4)).reshape(-1, feats)
    gate_f = gate.astype(jnp.float32)
    up_f = up.astype(jnp.float32)
    sig = jax.nn.sigmoid(gate_f)
    act = gate_f * sig
    hidden = (act * up_f).astype(jnp.bfloat16)
    rows3 = out_rows.reshape(out_rows.shape[0], 2, half, feat_dev)
    cot_near = jnp.take(rows3, side, axis=1, mode="clip")
    cot_far = jnp.take(rows3, 1 - side, axis=1, mode="clip")
    cot_far = jnp.take(cot_far, far_src, axis=1, mode="clip")
    d_hidden = jnp.einsum(
        "tsd,sfd->tf", cot_near, near, preferred_element_type=jnp.float32
    ) + jnp.einsum("tsd,sfd->tf", cot_far, far, preferred_element_type=jnp.float32)
    d_up = (d_hidden * act).astype(jnp.bfloat16)
    d_gate = (d_hidden * up_f * sig * (1.0 + gate_f * (1.0 - sig))).astype(jnp.bfloat16)
    selector = (language[None, :] == jnp.arange(variants, dtype=jnp.int32)[:, None]).astype(
        jnp.bfloat16
    )
    partial_term = lax.dot_general(
        hidden, out_rows, (((0,), (0,)), ((), ())), preferred_element_type=jnp.float32
    ).astype(jnp.bfloat16)
    pieces = lax.all_to_all(
        partial_term.reshape(ff_dev, groups, feat_dev),
        DP,
        split_axis=1,
        concat_axis=1,
        tiled=True,
    )
    d_weight = jnp.einsum("lg,fgd->lfd", selector, pieces, preferred_element_type=jnp.float32)
    return (d_gate, d_up, d_weight)


def solution(mesh):
    sub = Mesh(mesh.devices.reshape(2, 2, 4, 2, 4, 2), DP + TP)
    return jax.shard_map(
        shards,
        mesh=sub,
        in_specs=(
            P(DP + TP, None),
            P(DP, TP),
            P(DP, TP),
            P(None, TP, DP),
            P(),
        ),
        out_specs=(P(DP, TP), P(DP, TP), P(None, TP, DP)),
        check_vma=False,
    )
```

```python
import jax
import jax.numpy as jnp
from jax import lax
from jax.experimental import pallas as pl
from jax.experimental.pallas import tpu as pltpu
from jax.sharding import Mesh
from jax.sharding import PartitionSpec as P

DP = ("zh2", "zl2", "x")
HALF = ("zl2", "x")
TP = ("zh", "y", "c")


def _combine_kernel(lang_ref, x_ref, o_ref):
    o_ref[...] = jnp.zeros_like(o_ref)
    top = o_ref.shape[0] - 1
    for g in range(x_ref.shape[0]):
        lang = jnp.minimum(jnp.maximum(lang_ref[g], 0), top)
        o_ref[lang] += x_ref[g].astype(jnp.float32)


def combine(language, pieces, variants):
    groups, ff_dev, feat_dev = pieces.shape
    tile = 128
    return pl.pallas_call(
        _combine_kernel,
        out_shape=jax.ShapeDtypeStruct((variants, ff_dev, feat_dev), jnp.float32),
        grid_spec=pltpu.PrefetchScalarGridSpec(
            num_scalar_prefetch=1,
            grid=(ff_dev // tile,),
            in_specs=[pl.BlockSpec((groups, tile, feat_dev), lambda i, lang: (0, i, 0))],
            out_specs=pl.BlockSpec((variants, tile, feat_dev), lambda i, lang: (0, i, 0)),
        ),
        cost_estimate=pl.CostEstimate(
            flops=groups * ff_dev * feat_dev,
            transcendentals=0,
            bytes_accessed=pieces.size * 2 + variants * ff_dev * feat_dev * 4,
        ),
    )(language, pieces)


def shards(cotangent, gate, up, w_down, language):
    groups = lax.axis_size(DP)
    variants = w_down.shape[0]
    ff_dev = w_down.shape[1]
    feat_dev = w_down.shape[2]
    rows_dev, feats = cotangent.shape
    cores = lax.axis_size("c")
    partner = lax.ppermute(cotangent, "zh", [(0, 1), (1, 0)])
    half = lax.axis_size(HALF)
    side = lax.axis_index("zh2")
    lang = language.reshape(2, half)
    own_langs = jnp.take(lang, side, axis=0, mode="clip")
    own_slabs = jnp.take(w_down, own_langs, axis=0, mode="clip")
    partner, own_slabs = lax.optimization_barrier((partner, own_slabs))
    near = lax.all_to_all(own_slabs, HALF, split_axis=0, concat_axis=0, tiled=True)
    block = lax.ppermute(w_down, "zh2", [(0, 1), (1, 0)])
    relay = jnp.take(block, own_langs, axis=0, mode="clip")
    far = lax.all_to_all(relay, HALF, split_axis=0, concat_axis=0, tiled=True)
    first = lax.axis_index("zh") == 0
    pair = jnp.where(first, jnp.stack([cotangent, partner]), jnp.stack([partner, cotangent]))
    ring = lax.axis_size("y")
    me_y = lax.axis_index("y")
    got = [pair]
    for shift in range(1, ring):
        got.append(lax.ppermute(pair, "y", [(i, (i + shift) % ring) for i in range(ring)]))
    by_y = jnp.stack(got)
    order = (me_y - jnp.arange(ring)) % ring
    by_y = jnp.take(by_y, jnp.argsort(order), axis=0, mode="clip")
    other = lax.ppermute(by_y, "c", [(0, 1), (1, 0)])
    first_c = lax.axis_index("c") == 0
    both = jnp.where(first_c, jnp.stack([by_y, other]), jnp.stack([other, by_y]))
    out_rows = jnp.transpose(both, (2, 1, 0, 3, 4)).reshape(-1, feats)
    gate_f = gate.astype(jnp.float32)
    up_f = up.astype(jnp.float32)
    sig = jax.nn.sigmoid(gate_f)
    act = gate_f * sig
    hidden = (act * up_f).astype(jnp.bfloat16)
    rows3 = out_rows.reshape(out_rows.shape[0], 2, half, feat_dev)
    cot_near = jnp.take(rows3, side, axis=1, mode="clip")
    cot_far = jnp.take(rows3, 1 - side, axis=1, mode="clip")
    d_hidden = jnp.einsum(
        "tsd,sfd->tf", cot_near, near, preferred_element_type=jnp.float32
    ) + jnp.einsum("tsd,sfd->tf", cot_far, far, preferred_element_type=jnp.float32)
    d_up = (d_hidden * act).astype(jnp.bfloat16)
    d_gate = (d_hidden * up_f * sig * (1.0 + gate_f * (1.0 - sig))).astype(jnp.bfloat16)
    partial_term = lax.dot_general(
        hidden, out_rows, (((0,), (0,)), ((), ())), preferred_element_type=jnp.float32
    ).astype(jnp.bfloat16)
    pieces = jnp.transpose(partial_term.reshape(ff_dev, groups, feat_dev), (1, 0, 2))
    pieces = lax.all_to_all(pieces, DP, split_axis=0, concat_axis=0, tiled=True)
    d_weight = combine(language, pieces, variants)
    return (d_gate, d_up, d_weight)


def solution(mesh):
    sub = Mesh(mesh.devices.reshape(2, 2, 4, 2, 4, 2), DP + TP)
    return jax.shard_map(
        shards,
        mesh=sub,
        in_specs=(
            P(DP + TP, None),
            P(DP, TP),
            P(DP, TP),
            P(None, TP, DP),
            P(),
        ),
        out_specs=(P(DP, TP), P(DP, TP), P(None, TP, DP)),
        check_vma=False,
    )
```

```python
import jax
import jax.numpy as jnp
from jax import lax
from jax.sharding import Mesh
from jax.sharding import PartitionSpec as P

DP = ("zh2", "zl2", "x")
HALF = ("zl2", "x")
TP = ("zh", "y", "c")


def shards(cotangent, gate, up, w_down, language):
    groups = lax.axis_size(DP)
    variants = w_down.shape[0]
    ff_dev = w_down.shape[1]
    feat_dev = w_down.shape[2]
    rows_dev, feats = cotangent.shape
    cores = lax.axis_size("c")
    partner = lax.ppermute(cotangent, "zh", [(0, 1), (1, 0)])
    half = lax.axis_size(HALF)
    side = lax.axis_index("zh2")
    lang = language.reshape(2, half)
    own_langs = jnp.take(lang, side, axis=0, mode="clip")
    own_slabs = jnp.take(w_down, own_langs, axis=0, mode="clip")
    near = lax.all_to_all(own_slabs, HALF, split_axis=0, concat_axis=0, tiled=True)
    block = lax.ppermute(w_down, "zh2", [(0, 1), (1, 0)])
    relay = jnp.take(block, own_langs, axis=0, mode="clip")
    far = lax.all_to_all(relay, HALF, split_axis=0, concat_axis=0, tiled=True)
    first = lax.axis_index("zh") == 0
    pair = jnp.where(first, jnp.stack([cotangent, partner]), jnp.stack([partner, cotangent]))
    ring = lax.axis_size("y")
    me_y = lax.axis_index("y")
    got = [pair]
    for shift in range(1, ring):
        got.append(lax.ppermute(pair, "y", [(i, (i + shift) % ring) for i in range(ring)]))
    by_y = jnp.stack(got)
    order = (me_y - jnp.arange(ring)) % ring
    by_y = jnp.take(by_y, jnp.argsort(order), axis=0, mode="clip")
    other = lax.ppermute(by_y, "c", [(0, 1), (1, 0)])
    first_c = lax.axis_index("c") == 0
    both = jnp.where(first_c, jnp.stack([by_y, other]), jnp.stack([other, by_y]))
    out_rows = jnp.transpose(both, (2, 1, 0, 3, 4)).reshape(-1, feats)
    gate_f = gate.astype(jnp.float32)
    up_f = up.astype(jnp.float32)
    sig = jax.nn.sigmoid(gate_f)
    act = gate_f * sig
    hidden = (act * up_f).astype(jnp.bfloat16)
    rows3 = out_rows.reshape(out_rows.shape[0], 2, half, feat_dev)
    cot_near = jnp.take(rows3, side, axis=1, mode="clip")
    cot_far = jnp.take(rows3, 1 - side, axis=1, mode="clip")
    d_hidden = jnp.einsum(
        "tsd,sfd->tf", cot_near, near, preferred_element_type=jnp.float32
    ) + jnp.einsum("tsd,sfd->tf", cot_far, far, preferred_element_type=jnp.float32)
    d_up = (d_hidden * act).astype(jnp.bfloat16)
    d_gate = (d_hidden * up_f * sig * (1.0 + gate_f * (1.0 - sig))).astype(jnp.bfloat16)
    selector = (language[None, :] == jnp.arange(variants, dtype=jnp.int32)[:, None]).astype(
        jnp.bfloat16
    )
    partial_term = lax.dot_general(
        hidden, out_rows, (((0,), (0,)), ((), ())), preferred_element_type=jnp.float32
    ).astype(jnp.bfloat16)
    pieces = lax.all_to_all(
        partial_term.reshape(ff_dev, groups, feat_dev),
        DP,
        split_axis=1,
        concat_axis=1,
        tiled=True,
    )
    d_weight = jnp.einsum("lg,fgd->lfd", selector, pieces, preferred_element_type=jnp.float32)
    return (d_gate, d_up, d_weight)


def solution(mesh):
    sub = Mesh(mesh.devices.reshape(2, 2, 4, 2, 4, 2), DP + TP)
    return jax.shard_map(
        shards,
        mesh=sub,
        in_specs=(
            P(DP + TP, None),
            P(DP, TP),
            P(DP, TP),
            P(None, TP, DP),
            P(),
        ),
        out_specs=(P(DP, TP), P(DP, TP), P(None, TP, DP)),
        check_vma=False,
    )
```

```python
import jax
import jax.numpy as jnp
from jax import lax
from jax.sharding import Mesh
from jax.sharding import PartitionSpec as P

DP = ("zh2", "zl2", "x")
HALF = ("zl2", "x")
TP = ("zh", "y", "c")


def shards(cotangent, gate, up, w_down, language):
    groups = lax.axis_size(DP)
    variants = w_down.shape[0]
    ff_dev = w_down.shape[1]
    feat_dev = w_down.shape[2]
    rows_dev, feats = cotangent.shape
    cores = lax.axis_size("c")
    partner = lax.ppermute(cotangent, "zh", [(0, 1), (1, 0)])
    half = lax.axis_size(HALF)
    side = lax.axis_index("zh2")
    lang = language.reshape(2, half)
    own_langs = jnp.take(lang, side, axis=0, mode="clip")
    own_slabs = jnp.take(w_down, own_langs, axis=0, mode="clip")
    near = lax.all_to_all(own_slabs, HALF, split_axis=0, concat_axis=0, tiled=True)
    block = lax.ppermute(w_down, "zh2", [(0, 1), (1, 0)])
    partner, block = lax.optimization_barrier((partner, block))
    relay = jnp.take(block, own_langs, axis=0, mode="clip")
    far = lax.all_to_all(relay, HALF, split_axis=0, concat_axis=0, tiled=True)
    first = lax.axis_index("zh") == 0
    pair = jnp.where(first, jnp.stack([cotangent, partner]), jnp.stack([partner, cotangent]))
    ring = lax.axis_size("y")
    me_y = lax.axis_index("y")
    got = [pair]
    for shift in range(1, ring):
        got.append(lax.ppermute(pair, "y", [(i, (i + shift) % ring) for i in range(ring)]))
    by_y = jnp.stack(got)
    order = (me_y - jnp.arange(ring)) % ring
    by_y = jnp.take(by_y, jnp.argsort(order), axis=0, mode="clip")
    other = lax.ppermute(by_y, "c", [(0, 1), (1, 0)])
    first_c = lax.axis_index("c") == 0
    both = jnp.where(first_c, jnp.stack([by_y, other]), jnp.stack([other, by_y]))
    out_rows = jnp.transpose(both, (2, 1, 0, 3, 4)).reshape(-1, feats)
    gate_f = gate.astype(jnp.float32)
    up_f = up.astype(jnp.float32)
    sig = jax.nn.sigmoid(gate_f)
    act = gate_f * sig
    hidden = (act * up_f).astype(jnp.bfloat16)
    rows3 = out_rows.reshape(out_rows.shape[0], 2, half, feat_dev)
    cot_near = jnp.take(rows3, side, axis=1, mode="clip")
    cot_far = jnp.take(rows3, 1 - side, axis=1, mode="clip")
    d_hidden = jnp.einsum(
        "tsd,sfd->tf", cot_near, near, preferred_element_type=jnp.float32
    ) + jnp.einsum("tsd,sfd->tf", cot_far, far, preferred_element_type=jnp.float32)
    d_up = (d_hidden * act).astype(jnp.bfloat16)
    d_gate = (d_hidden * up_f * sig * (1.0 + gate_f * (1.0 - sig))).astype(jnp.bfloat16)
    selector = (language[None, :] == jnp.arange(variants, dtype=jnp.int32)[:, None]).astype(
        jnp.bfloat16
    )
    partial_term = lax.dot_general(
        hidden, out_rows, (((0,), (0,)), ((), ())), preferred_element_type=jnp.float32
    ).astype(jnp.bfloat16)
    pieces = lax.all_to_all(
        partial_term.reshape(ff_dev, groups, feat_dev),
        DP,
        split_axis=1,
        concat_axis=1,
        tiled=True,
    )
    d_weight = jnp.einsum("lg,fgd->lfd", selector, pieces, preferred_element_type=jnp.float32)
    return (d_gate, d_up, d_weight)


def solution(mesh):
    sub = Mesh(mesh.devices.reshape(2, 2, 4, 2, 4, 2), DP + TP)
    return jax.shard_map(
        shards,
        mesh=sub,
        in_specs=(
            P(DP + TP, None),
            P(DP, TP),
            P(DP, TP),
            P(None, TP, DP),
            P(),
        ),
        out_specs=(P(DP, TP), P(DP, TP), P(None, TP, DP)),
        check_vma=False,
    )
```

```python
import jax
import jax.numpy as jnp
from jax import lax
from jax.sharding import Mesh
from jax.sharding import PartitionSpec as P

DP = ("zh2", "zl2", "x")
HALF = ("zl2", "x")
TP = ("zh", "y", "c")


def shards(cotangent, gate, up, w_down, language):
    groups = lax.axis_size(DP)
    variants = w_down.shape[0]
    ff_dev = w_down.shape[1]
    feat_dev = w_down.shape[2]
    rows_dev, feats = cotangent.shape
    cores = lax.axis_size("c")
    partner = lax.ppermute(cotangent, "zh", [(0, 1), (1, 0)])
    half = lax.axis_size(HALF)
    side = lax.axis_index("zh2")
    lang = language.reshape(2, half)
    own_langs = jnp.take(lang, side, axis=0, mode="clip")
    own_slabs = jnp.take(w_down, own_langs, axis=0, mode="clip")
    partner, own_slabs = lax.optimization_barrier((partner, own_slabs))
    near = lax.all_to_all(own_slabs, HALF, split_axis=0, concat_axis=0, tiled=True)
    block = lax.ppermute(w_down, "zh2", [(0, 1), (1, 0)])
    relay = jnp.take(block, own_langs, axis=0, mode="clip")
    first = lax.axis_index("zh") == 0
    pair = jnp.where(first, jnp.stack([cotangent, partner]), jnp.stack([partner, cotangent]))
    ring = lax.axis_size("y")
    me_y = lax.axis_index("y")
    got = [pair]
    for shift in range(1, ring):
        got.append(lax.ppermute(pair, "y", [(i, (i + shift) % ring) for i in range(ring)]))
    by_y = jnp.stack(got)
    order = (me_y - jnp.arange(ring)) % ring
    by_y = jnp.take(by_y, jnp.argsort(order), axis=0, mode="clip")
    other = lax.ppermute(by_y, "c", [(0, 1), (1, 0)])
    first_c = lax.axis_index("c") == 0
    both = jnp.where(first_c, jnp.stack([by_y, other]), jnp.stack([other, by_y]))
    out_rows = jnp.transpose(both, (2, 1, 0, 3, 4)).reshape(-1, feats)
    gate_f = gate.astype(jnp.float32)
    up_f = up.astype(jnp.float32)
    sig = jax.nn.sigmoid(gate_f)
    act = gate_f * sig
    hidden = (act * up_f).astype(jnp.bfloat16)
    partial_term = lax.dot_general(
        hidden, out_rows, (((0,), (0,)), ((), ())), preferred_element_type=jnp.float32
    ).astype(jnp.bfloat16)
    pieces = jnp.transpose(partial_term.reshape(ff_dev, groups, feat_dev), (1, 0, 2))
    own_start = side * half
    send = lax.dynamic_update_slice(pieces, relay, (own_start, 0, 0))
    got = lax.all_to_all(send, DP, split_axis=0, concat_axis=0, tiled=True)
    far = lax.dynamic_slice_in_dim(got, own_start, half, axis=0)
    own_pieces = lax.dynamic_slice_in_dim(pieces, own_start, half, axis=0)
    own_got = lax.all_to_all(own_pieces, HALF, split_axis=0, concat_axis=0, tiled=True)
    by_group = lax.dynamic_update_slice(got, own_got, (own_start, 0, 0))
    rows3 = out_rows.reshape(out_rows.shape[0], 2, half, feat_dev)
    cot_near = jnp.take(rows3, side, axis=1, mode="clip")
    cot_far = jnp.take(rows3, 1 - side, axis=1, mode="clip")
    d_hidden = jnp.einsum(
        "tsd,sfd->tf", cot_near, near, preferred_element_type=jnp.float32
    ) + jnp.einsum("tsd,sfd->tf", cot_far, far, preferred_element_type=jnp.float32)
    d_up = (d_hidden * act).astype(jnp.bfloat16)
    d_gate = (d_hidden * up_f * sig * (1.0 + gate_f * (1.0 - sig))).astype(jnp.bfloat16)
    selector = (language[None, :] == jnp.arange(variants, dtype=jnp.int32)[:, None]).astype(
        jnp.bfloat16
    )
    d_weight = jnp.einsum(
        "lg,gfd->lfd", selector, by_group, preferred_element_type=jnp.float32
    )
    return (d_gate, d_up, d_weight)


def solution(mesh):
    sub = Mesh(mesh.devices.reshape(2, 2, 4, 2, 4, 2), DP + TP)
    return jax.shard_map(
        shards,
        mesh=sub,
        in_specs=(
            P(DP + TP, None),
            P(DP, TP),
            P(DP, TP),
            P(None, TP, DP),
            P(),
        ),
        out_specs=(P(DP, TP), P(DP, TP), P(None, TP, DP)),
        check_vma=False,
    )
```

```python
import jax
import jax.numpy as jnp
from jax import lax
from jax.sharding import Mesh
from jax.sharding import PartitionSpec as P

DP = ("zh2", "zl2", "x")
HALF = ("zl2", "x")
TP = ("zh", "y", "c")


def shards(cotangent, gate, up, w_down, language):
    groups = lax.axis_size(DP)
    variants = w_down.shape[0]
    ff_dev = w_down.shape[1]
    feat_dev = w_down.shape[2]
    rows_dev, feats = cotangent.shape
    cores = lax.axis_size("c")
    partner = lax.ppermute(cotangent, "zh", [(0, 1), (1, 0)])
    half = lax.axis_size(HALF)
    side = lax.axis_index("zh2")
    lang = language.reshape(2, half)
    own_langs = jnp.take(lang, side, axis=0, mode="clip")
    own_slabs = jnp.take(w_down, own_langs, axis=0, mode="clip")
    partner, own_slabs = lax.optimization_barrier((partner, own_slabs))
    near = lax.all_to_all(own_slabs, HALF, split_axis=0, concat_axis=0, tiled=True)
    block = lax.ppermute(w_down, "zh2", [(0, 1), (1, 0)])
    relay = jnp.take(block, own_langs, axis=0, mode="clip")
    far = lax.all_to_all(relay, HALF, split_axis=0, concat_axis=0, tiled=True)
    first = lax.axis_index("zh") == 0
    pair = jnp.where(first, jnp.stack([cotangent, partner]), jnp.stack([partner, cotangent]))
    ring = lax.axis_size("y")
    me_y = lax.axis_index("y")
    got = [pair]
    for shift in range(1, ring):
        got.append(lax.ppermute(pair, "y", [(i, (i + shift) % ring) for i in range(ring)]))
    by_y = jnp.stack(got)
    order = (me_y - jnp.arange(ring)) % ring
    by_y = jnp.take(by_y, jnp.argsort(order), axis=0, mode="clip")
    other = lax.ppermute(by_y, "c", [(0, 1), (1, 0)])
    first_c = lax.axis_index("c") == 0
    both = jnp.where(first_c, jnp.stack([by_y, other]), jnp.stack([other, by_y]))
    out_rows = jnp.transpose(both, (2, 1, 0, 3, 4)).reshape(-1, feats)
    gate_f = gate.astype(jnp.float32)
    up_f = up.astype(jnp.float32)
    sig = jax.nn.sigmoid(gate_f)
    act = gate_f * sig
    hidden = (act * up_f).astype(jnp.bfloat16)
    rows3 = out_rows.reshape(out_rows.shape[0], 2, half, feat_dev)
    cot_near = jnp.take(rows3, side, axis=1, mode="clip")
    cot_far = jnp.take(rows3, 1 - side, axis=1, mode="clip")
    d_hidden = jnp.einsum(
        "tsd,sfd->tf", cot_near, near, preferred_element_type=jnp.float32
    ) + jnp.einsum("tsd,sfd->tf", cot_far, far, preferred_element_type=jnp.float32)
    d_up = (d_hidden * act).astype(jnp.bfloat16)
    d_gate = (d_hidden * up_f * sig * (1.0 + gate_f * (1.0 - sig))).astype(jnp.bfloat16)
    selector = (language[None, :] == jnp.arange(variants, dtype=jnp.int32)[:, None]).astype(
        jnp.bfloat16
    )
    partial_t = lax.dot_general(
        out_rows, hidden, (((0,), (0,)), ((), ())), preferred_element_type=jnp.float32
    ).astype(jnp.bfloat16)
    pieces = lax.all_to_all(
        partial_t.reshape(groups, feat_dev, ff_dev), DP, split_axis=0, concat_axis=0, tiled=True
    )
    d_weight = jnp.einsum("lg,gdf->lfd", selector, pieces, preferred_element_type=jnp.float32)
    return (d_gate, d_up, d_weight)


def solution(mesh):
    sub = Mesh(mesh.devices.reshape(2, 2, 4, 2, 4, 2), DP + TP)
    return jax.shard_map(
        shards,
        mesh=sub,
        in_specs=(
            P(DP + TP, None),
            P(DP, TP),
            P(DP, TP),
            P(None, TP, DP),
            P(),
        ),
        out_specs=(P(DP, TP), P(DP, TP), P(None, TP, DP)),
        check_vma=False,
    )
```

```python
import jax
import jax.numpy as jnp
from jax import lax
from jax.sharding import Mesh
from jax.sharding import PartitionSpec as P

DP = ("zh2", "zl2", "x")
HALF = ("zl2", "x")
TP = ("zh", "y", "c")


def shards(cotangent, gate, up, w_down, language):
    groups = lax.axis_size(DP)
    variants = w_down.shape[0]
    ff_dev = w_down.shape[1]
    feat_dev = w_down.shape[2]
    rows_dev, feats = cotangent.shape
    cores = lax.axis_size("c")
    partner = lax.ppermute(cotangent, "zh", [(0, 1), (1, 0)])
    half = lax.axis_size(HALF)
    side = lax.axis_index("zh2")
    lang = language.reshape(2, half)
    own_langs = jnp.take(lang, side, axis=0, mode="clip")
    own_slabs = jnp.take(w_down, own_langs, axis=0, mode="clip")
    partner, own_slabs = lax.optimization_barrier((partner, own_slabs))
    near = lax.all_to_all(own_slabs, HALF, split_axis=0, concat_axis=0, tiled=True)
    block = lax.ppermute(w_down, "zh2", [(0, 1), (1, 0)])
    relay = jnp.take(block, own_langs, axis=0, mode="clip")
    far = lax.all_to_all(relay, HALF, split_axis=0, concat_axis=0, tiled=True)
    first = lax.axis_index("zh") == 0
    pair = jnp.where(first, jnp.stack([cotangent, partner]), jnp.stack([partner, cotangent]))
    ring = lax.axis_size("y")
    me_y = lax.axis_index("y")
    got = [pair]
    for shift in range(1, ring):
        got.append(lax.ppermute(pair, "y", [(i, (i + shift) % ring) for i in range(ring)]))
    by_y = jnp.stack(got)
    order = (me_y - jnp.arange(ring)) % ring
    by_y = jnp.take(by_y, jnp.argsort(order), axis=0, mode="clip")
    other = lax.ppermute(by_y, "c", [(0, 1), (1, 0)])
    first_c = lax.axis_index("c") == 0
    both = jnp.where(first_c, jnp.stack([by_y, other]), jnp.stack([other, by_y]))
    out_rows = jnp.transpose(both, (2, 1, 0, 3, 4)).reshape(-1, feats)
    gate_f = gate.astype(jnp.float32)
    up_f = up.astype(jnp.float32)
    sig = jax.nn.sigmoid(gate_f)
    act = gate_f * sig
    hidden = (act * up_f).astype(jnp.bfloat16)
    rows3 = out_rows.reshape(out_rows.shape[0], 2, half, feat_dev)
    cot_near = jnp.take(rows3, side, axis=1, mode="clip")
    cot_far = jnp.take(rows3, 1 - side, axis=1, mode="clip")
    d_hidden = jnp.einsum(
        "tsd,sfd->tf", cot_near, near, preferred_element_type=jnp.float32
    ) + jnp.einsum("tsd,sfd->tf", cot_far, far, preferred_element_type=jnp.float32)
    d_up = (d_hidden * act).astype(jnp.bfloat16)
    d_gate = (d_hidden * up_f * sig * (1.0 + gate_f * (1.0 - sig))).astype(jnp.bfloat16)
    selector = (language[None, :] == jnp.arange(variants, dtype=jnp.int32)[:, None]).astype(
        jnp.bfloat16
    )
    partial_term = lax.dot_general(
        hidden, out_rows, (((0,), (0,)), ((), ())), preferred_element_type=jnp.float32
    ).astype(jnp.bfloat16)
    pieces = lax.all_to_all(
        partial_term.reshape(ff_dev, groups, feat_dev),
        DP,
        split_axis=1,
        concat_axis=1,
        tiled=True,
    )
    by_group = jnp.transpose(pieces, (1, 0, 2))
    d_weight = jnp.sum(selector[:, :, None, None] * by_group[None], axis=1, dtype=jnp.float32)
    return (d_gate, d_up, d_weight)


def solution(mesh):
    sub = Mesh(mesh.devices.reshape(2, 2, 4, 2, 4, 2), DP + TP)
    return jax.shard_map(
        shards,
        mesh=sub,
        in_specs=(
            P(DP + TP, None),
            P(DP, TP),
            P(DP, TP),
            P(None, TP, DP),
            P(),
        ),
        out_specs=(P(DP, TP), P(DP, TP), P(None, TP, DP)),
        check_vma=False,
    )
```

```python
import jax
import jax.numpy as jnp
from jax import lax
from jax.sharding import Mesh
from jax.sharding import PartitionSpec as P

DP = ("zh2", "zl2", "x")
HALF = ("zl2", "x")
TP = ("zh", "y", "c")


def shards(cotangent, gate, up, w_down, language):
    groups = lax.axis_size(DP)
    variants = w_down.shape[0]
    ff_dev = w_down.shape[1]
    feat_dev = w_down.shape[2]
    rows_dev, feats = cotangent.shape
    cores = lax.axis_size("c")
    partner = lax.ppermute(cotangent, "zh", [(0, 1), (1, 0)])
    half = lax.axis_size(HALF)
    side = lax.axis_index("zh2")
    lang = language.reshape(2, half)
    own_langs = jnp.take(lang, side, axis=0, mode="clip")
    own_slabs = jnp.take(w_down, own_langs, axis=0, mode="clip")
    partner, own_slabs = lax.optimization_barrier((partner, own_slabs))
    near = lax.all_to_all(own_slabs, HALF, split_axis=0, concat_axis=0, tiled=True)
    block = lax.ppermute(w_down, "zh2", [(0, 1), (1, 0)])
    relay = jnp.take(block, own_langs, axis=0, mode="clip")
    far = lax.all_to_all(relay, HALF, split_axis=0, concat_axis=0, tiled=True)
    first = lax.axis_index("zh") == 0
    pair = jnp.where(first, jnp.stack([cotangent, partner]), jnp.stack([partner, cotangent]))
    ring = lax.axis_size("y")
    me_y = lax.axis_index("y")
    got = [pair]
    for shift in range(1, ring):
        got.append(lax.ppermute(pair, "y", [(i, (i + shift) % ring) for i in range(ring)]))
    by_y = jnp.stack(got)
    order = (me_y - jnp.arange(ring)) % ring
    by_y = jnp.take(by_y, jnp.argsort(order), axis=0, mode="clip")
    other = lax.ppermute(by_y, "c", [(0, 1), (1, 0)])
    first_c = lax.axis_index("c") == 0
    both = jnp.where(first_c, jnp.stack([by_y, other]), jnp.stack([other, by_y]))
    out_rows = jnp.transpose(both, (2, 1, 0, 3, 4)).reshape(-1, feats)
    gate_f = gate.astype(jnp.float32)
    up_f = up.astype(jnp.float32)
    sig = jax.nn.sigmoid(gate_f)
    act = gate_f * sig
    hidden = (act * up_f).astype(jnp.bfloat16)
    rows3 = out_rows.reshape(out_rows.shape[0], 2, half, feat_dev)
    cot_near = jnp.take(rows3, side, axis=1, mode="clip")
    cot_far = jnp.take(rows3, 1 - side, axis=1, mode="clip")
    d_hidden = jnp.einsum(
        "tsd,sfd->tf", cot_near, near, preferred_element_type=jnp.float32
    ) + jnp.einsum("tsd,sfd->tf", cot_far, far, preferred_element_type=jnp.float32)
    d_up = (d_hidden * act).astype(jnp.bfloat16)
    d_gate = (d_hidden * up_f * sig * (1.0 + gate_f * (1.0 - sig))).astype(jnp.bfloat16)
    selector = (language[None, :] == jnp.arange(variants, dtype=jnp.int32)[:, None]).astype(
        jnp.bfloat16
    )
    partial_term = lax.dot_general(
        hidden, out_rows, (((0,), (0,)), ((), ())), preferred_element_type=jnp.float32
    ).astype(jnp.bfloat16)
    pieces = lax.all_to_all(
        partial_term.reshape(ff_dev, groups, feat_dev),
        DP,
        split_axis=1,
        concat_axis=1,
        tiled=True,
    )
    d_fld = jnp.sum(selector[None, :, :, None] * pieces[:, None], axis=2, dtype=jnp.float32)
    d_weight = jnp.transpose(d_fld, (1, 0, 2))
    return (d_gate, d_up, d_weight)


def solution(mesh):
    sub = Mesh(mesh.devices.reshape(2, 2, 4, 2, 4, 2), DP + TP)
    return jax.shard_map(
        shards,
        mesh=sub,
        in_specs=(
            P(DP + TP, None),
            P(DP, TP),
            P(DP, TP),
            P(None, TP, DP),
            P(),
        ),
        out_specs=(P(DP, TP), P(DP, TP), P(None, TP, DP)),
        check_vma=False,
    )
```
